128 devices in a mesh: node: 8 (over x, core), dev: 16 (over z, y).
Axes of the slice: x: 4, y: 4, z: 4, core: 2. Of those that a mesh axis runs over, the one named last changes fastest.
Arguments:
- tokens: bfloat16 [32768, 7168], P(('node', 'dev')), may hold values from -6 to 6
- grad_out: bfloat16 [32768, 7168], P(('node', 'dev')), may hold values from -1.796875 to 1.796875
- router_gates: bfloat16 [32768, 8], P(('node', 'dev')), may hold values from 0.049804688 to 1
- expert_ids: int32 [32768, 8], P(('node', 'dev')), may hold values from 0 to 255, as said below
- slot_plan: int32 [256, 2], replicated, may hold values from 0 to 16, as said below
- w_gate: bfloat16 [8, 7168, 2048], P(None, 'dev', 'node'), may hold values from -0.0625 to 0.0625
- w_up: bfloat16 [8, 7168, 2048], P(None, 'dev', 'node'), may hold values from -0.0625 to 0.0625
- w_down: bfloat16 [8, 2048, 7168], P(None, 'node', 'dev'), may hold values from -0.125 to 0.125
Outputs:
- grad_tokens: bfloat16 [32768, 7168], P(('node', 'dev'))
- grad_gates: float32 [32768, 8], P(('node', 'dev'))
- grad_w_gate: bfloat16 [8, 7168, 2048], P(None, 'dev', 'node')
- grad_w_up: bfloat16 [8, 7168, 2048], P(None, 'dev', 'node')
- grad_w_down: bfloat16 [8, 2048, 7168], P(None, 'node', 'dev')
The draws below stay inside these ranges and needn't reach their ends.
Inputs may be any that keep to these rules, and one draw needn't show every extreme that they name: `expert_ids`: each token names 8 different experts. Within one block of 256 tokens (the tokens of one device), at most 4 pairs name any one expert that has slots, and in every draw one expert that has slots is named exactly 2 * 2 times in every block. `slot_plan`: exactly 8 rows hold slots: each such row holds two different slots, and every slot 0 .. 15 stands in exactly one row. Every entry of the other rows equals 16.
All inputs are finite; a program needn't handle non-finite values.
Results may differ from the reference program's by a relative error of at most 0.0059.
Values may be sent and summed in bfloat16 or wider, within the bound.
No kernel may reach another device: no remote copies, remote signals or barrier semaphores. Data moves between devices by JAX's collectives and lax.ppermute only.
A program may use at most 128 MiB of HBM per device.

```python
import jax
import jax.numpy as jnp
from jax import lax

D = 7168
F = 2048
EXPERTS = 256
TOP = 8
REPS = 2
TOK_DEV = 256
CAP = 2
SLOTS = 16
ROUND = 8
TOKENS = 32768


def routing_tables(key):
    sub_keys = [jax.random.fold_in(key, 7001 + number) for number in range(8)]
    block_count = TOKENS // TOK_DEV
    expert_order = jax.random.permutation(sub_keys[0], EXPERTS).astype(jnp.int32)
    round_ids = expert_order[:ROUND]
    slot_order = jax.random.permutation(sub_keys[1], SLOTS).astype(jnp.int32).reshape(ROUND, REPS)
    slot_plan = jnp.full((EXPERTS, REPS), SLOTS, jnp.int32).at[round_ids].set(slot_order)
    full_expert = jax.random.randint(sub_keys[2], (), 0, ROUND)
    picks = jax.random.randint(sub_keys[3], (block_count, ROUND), 0, 2 * CAP + 1)
    picks = jnp.where(jnp.arange(ROUND)[None, :] == full_expert, 2 * CAP, picks)
    scores = jax.random.randint(sub_keys[4], (block_count, ROUND, TOK_DEV), 0, 1 << 20) * TOK_DEV + jnp.arange(TOK_DEV, dtype=jnp.int32)
    standing = jnp.argsort(jnp.argsort(scores, axis=-1), axis=-1)
    chosen = (standing < picks[:, :, None]).transpose(0, 2, 1).reshape(TOKENS, ROUND)
    placing = jnp.cumsum(chosen.astype(jnp.int32), axis=1) - 1
    taken = jnp.sum(chosen.astype(jnp.int32), axis=1)
    column = jnp.arange(TOP, dtype=jnp.int32)
    landing = chosen[:, None, :] & (placing[:, None, :] == column[None, :, None])
    round_pick = jnp.sum(jnp.where(landing, round_ids[None, None, :], 0), axis=-1)
    others = EXPERTS - ROUND
    offset = jax.random.randint(sub_keys[5], (TOKENS, 1), 0, others)
    filler = expert_order[ROUND + (offset + column[None, :] - taken[:, None]) % others]
    picked = jnp.where(column[None, :] < taken[:, None], round_pick, filler)
    shuffle = jax.random.randint(sub_keys[6], (TOKENS, TOP), 0, 1 << 20) * TOP + column[None, :]
    column_order = jnp.argsort(shuffle, axis=1)
    expert_ids = jnp.take_along_axis(picked, column_order, axis=1).astype(jnp.int32)
    return (expert_ids, slot_plan)


def draw_expert_ids(key, part):
    return routing_tables(key)[0]


def draw_slot_plan(key, part):
    return routing_tables(key)[1]


def steps_of(stream_key, dims, cuts, least, high):
    factor_of = 1.0
    for axis_at, blocks in cuts:
        steps = jax.random.uniform(jax.random.fold_in(jax.random.fold_in(stream_key, 6), axis_at), (blocks,), jnp.float32, least / len(cuts), high / len(cuts))
        factor_of = factor_of * jnp.repeat(jnp.exp(steps), dims[axis_at] // blocks).reshape((-1,) + (1,) * (len(dims) - 1 - axis_at))
    return factor_of


def noise(key, shape, scale, limit, pieces=(), held_as=jnp.bfloat16):
    values = scale * jax.random.normal(key, shape, jnp.float32)
    if pieces:
        values = values * steps_of(key, shape, pieces, -0.22, 0.18)
    return jnp.clip(values, -limit, limit).astype(held_as)


def setup_inputs(seed: int = 0) -> dict:
    streams_of = jax.random.split(jax.random.key(seed), 9)
    return {
        "tokens": noise(streams_of[0], (TOKENS, D), 1.0, 6.0, ((0, 128),)),
        "grad_out": noise(streams_of[1], (TOKENS, D), 0.3, 1.796875, ((0, 128),)),
        "router_gates": jnp.clip(0.049804688 + 0.9501953 * jax.random.uniform(streams_of[2], (TOKENS, TOP), jnp.float32) ** steps_of(streams_of[2], (TOKENS, TOP), ((0, 128),), -0.2, 0.2), 0.049804688, 1.0).astype(jnp.bfloat16),
        "expert_ids": draw_expert_ids(jax.random.fold_in(streams_of[8], 71), 0),
        "slot_plan": draw_slot_plan(jax.random.fold_in(streams_of[8], 71), 0),
        "w_gate": noise(streams_of[5], (ROUND, D, F), D ** -0.5, 0.0625, ((1, 16), (2, 8))),
        "w_up": noise(streams_of[6], (ROUND, D, F), D ** -0.5, 0.0625, ((1, 16), (2, 8))),
        "w_down": noise(streams_of[7], (ROUND, F, D), F ** -0.5, 0.125, ((1, 8), (2, 16))),
    }


def served_pairs(expert_ids, slot_plan):
    block_count = TOKENS // TOK_DEV
    first_slot = slot_plan[:, 0][expert_ids].astype(jnp.int32)
    second_slot = slot_plan[:, 1][expert_ids].astype(jnp.int32)
    is_live = first_slot < SLOTS
    first_hot = (first_slot.reshape(block_count, TOK_DEV * TOP, 1) == jnp.arange(SLOTS, dtype=jnp.int32)).astype(jnp.int32)
    running = (jnp.cumsum(first_hot, axis=1) - 1).astype(jnp.int32)
    pair_order = jnp.sum(first_hot * running, axis=-1).astype(jnp.int32).reshape(TOKENS, TOP)
    pair_slot = jnp.where(pair_order % 2 == 0, first_slot, second_slot).astype(jnp.int32)
    block_index = (jnp.arange(TOKENS, dtype=jnp.int32) // TOK_DEV)[:, None]
    row_index = (block_index * CAP + pair_order // 2).astype(jnp.int32)
    return is_live, pair_slot, row_index


def reference(tokens, grad_out, router_gates, expert_ids, slot_plan, w_gate, w_up, w_down):
    is_live, pair_slot, row_index = served_pairs(expert_ids, slot_plan)
    row_total = (TOKENS // TOK_DEV) * CAP
    token_index = jnp.broadcast_to(jnp.arange(TOKENS, dtype=jnp.int32)[:, None], (TOKENS, TOP))
    pair_index = jnp.arange(TOKENS * TOP, dtype=jnp.int32).reshape(TOKENS, TOP)
    slot_key = jnp.where(is_live, pair_slot, SLOTS).astype(jnp.int32)
    row_token = jnp.full((SLOTS, row_total), -1, jnp.int32).at[slot_key, row_index].set(token_index, mode="drop")
    row_pair = jnp.full((SLOTS, row_total), -1, jnp.int32).at[slot_key, row_index].set(pair_index, mode="drop")
    in_round = (slot_plan[:, 0] < SLOTS).astype(jnp.int32)
    expert_rank = (jnp.cumsum(in_round) - 1).astype(jnp.int32)
    holder = jnp.any(slot_plan[:, :, None] == jnp.arange(SLOTS, dtype=jnp.int32), axis=1)
    slot_rank = jnp.sum(jnp.where(holder, expert_rank[:, None], 0), axis=0).astype(jnp.int32)
    rank_match = (in_round[:, None] > 0) & (expert_rank[:, None] == jnp.arange(ROUND, dtype=jnp.int32)[None, :])
    slot_pairs = jnp.sum(jnp.where(rank_match[:, :, None], slot_plan[:, None, :], 0), axis=0).astype(jnp.int32)
    flat_gates = router_gates.reshape(TOKENS * TOP)

    def one_slot(slot_id):
        live_token = row_token[slot_id]
        live_pair = row_pair[slot_id]
        present = live_token >= 0
        safe_token = jnp.maximum(live_token, 0)
        safe_pair = jnp.maximum(live_pair, 0)
        rows_x = jnp.where(present[:, None], tokens[safe_token], jnp.zeros((), tokens.dtype))
        rows_dy = jnp.where(present[:, None], grad_out[safe_token], jnp.zeros((), grad_out.dtype))
        rows_gate = jnp.where(present, flat_gates[safe_pair].astype(jnp.float32), jnp.zeros((), jnp.float32))
        expert_pos = slot_rank[slot_id]
        gate_w = w_gate[expert_pos]
        up_w = w_up[expert_pos]
        down_w = w_down[expert_pos]
        gate_pre = jnp.dot(rows_x, gate_w, preferred_element_type=jnp.float32)
        up_pre = jnp.dot(rows_x, up_w, preferred_element_type=jnp.float32)
        back_proj = jnp.dot(rows_dy, down_w.T, preferred_element_type=jnp.float32)
        sigmoid_gate = jax.nn.sigmoid(gate_pre)
        active = gate_pre * sigmoid_gate
        hidden = active * up_pre
        scaled_back = rows_gate[:, None] * back_proj
        d_gate = (scaled_back * up_pre * sigmoid_gate * (1.0 + gate_pre * (1.0 - sigmoid_gate))).astype(jnp.bfloat16)
        d_up = (scaled_back * active).astype(jnp.bfloat16)
        scaled_hidden = (rows_gate[:, None] * hidden).astype(jnp.bfloat16)
        gate_terms = jnp.sum(back_proj * hidden, axis=-1)
        grad_rows = jnp.dot(d_gate, gate_w.T, preferred_element_type=jnp.float32) + jnp.dot(d_up, up_w.T, preferred_element_type=jnp.float32)
        slot_gate = jnp.dot(rows_x.T, d_gate, preferred_element_type=jnp.float32).astype(jnp.bfloat16)
        slot_up = jnp.dot(rows_x.T, d_up, preferred_element_type=jnp.float32).astype(jnp.bfloat16)
        slot_down = jnp.dot(scaled_hidden.T, rows_dy, preferred_element_type=jnp.float32).astype(jnp.bfloat16)
        return slot_gate, slot_up, slot_down, grad_rows, gate_terms

    slot_gate, slot_up, slot_down, grad_rows, gate_terms = lax.map(one_slot, jnp.arange(SLOTS, dtype=jnp.int32))

    def pair_sum(slot_stack):
        left = slot_stack[slot_pairs[:, 0]].astype(jnp.float32)
        right = slot_stack[slot_pairs[:, 1]].astype(jnp.float32)
        return (left + right).astype(jnp.bfloat16)

    grad_w_gate = pair_sum(slot_gate)
    grad_w_up = pair_sum(slot_up)
    grad_w_down = pair_sum(slot_down)
    token_key = jnp.where(row_token >= 0, row_token, TOKENS).reshape(-1)
    pair_key = jnp.where(row_pair >= 0, row_pair, TOKENS * TOP).reshape(-1)
    grad_tokens = jnp.zeros((TOKENS, D), jnp.float32).at[token_key].add(grad_rows.reshape(-1, D), mode="drop").astype(jnp.bfloat16)
    grad_gates = jnp.zeros((TOKENS * TOP,), jnp.float32).at[pair_key].add(gate_terms.reshape(-1), mode="drop").reshape(TOKENS, TOP)
    return grad_tokens, grad_gates, grad_w_gate, grad_w_up, grad_w_down
```

```python
import jax
import jax.numpy as jnp
from jax import lax
from jax.sharding import PartitionSpec as P

TOP = 8
CAP = 2
REPS = 2


def routing(expert_ids, slot_plan, slot_count, round_total):
    expert_count = slot_plan.shape[0]
    in_round = (slot_plan[:, 0] < slot_count).astype(jnp.int32)
    expert_rank = jnp.cumsum(in_round) - 1
    rank_match = (in_round[:, None] > 0) & (
        expert_rank[:, None] == jnp.arange(round_total, dtype=jnp.int32)[None, :]
    )
    hot_ids = jnp.sum(
        jnp.where(rank_match, jnp.arange(expert_count, dtype=jnp.int32)[:, None], 0), axis=0
    )
    match = expert_ids[:, :, None] == hot_ids[None, None, :]
    named = jnp.sum(match.astype(jnp.int32), axis=1)
    tok_rows = expert_ids.shape[0]
    earlier = (
        jnp.arange(tok_rows, dtype=jnp.int32)[None, :] < jnp.arange(tok_rows, dtype=jnp.int32)[:, None]
    ).astype(jnp.bfloat16)
    before = jnp.dot(earlier, named.astype(jnp.bfloat16), preferred_element_type=jnp.float32).astype(
        jnp.int32
    )
    rank_ids = jnp.arange(round_total, dtype=jnp.int32)[None, :]
    column = REPS * rank_ids + before % REPS
    target = column * CAP + before // REPS
    return match, named, target


def local(tokens, grad_out, router_gates, expert_ids, slot_plan, w_gate, w_up, w_down):
    slot_count = lax.axis_size("dev")
    tok_rows, model_width = tokens.shape
    hidden_width = w_gate.shape[2]
    round_total = w_gate.shape[0]
    row_slots = slot_count * CAP
    chunk = model_width // slot_count

    send_wg = jnp.broadcast_to(w_gate[:, None], (round_total, REPS) + w_gate.shape[1:]).reshape(
        slot_count, chunk, hidden_width
    )
    send_wu = jnp.broadcast_to(w_up[:, None], (round_total, REPS) + w_up.shape[1:]).reshape(
        slot_count, chunk, hidden_width
    )
    down_t = jnp.swapaxes(w_down, 1, 2)
    send_wd = jnp.broadcast_to(down_t[:, None], (round_total, REPS) + down_t.shape[1:]).reshape(
        slot_count, chunk, hidden_width
    )
    slot_gate = lax.all_to_all(send_wg, "dev", 0, 0, tiled=True).reshape(model_width, hidden_width)
    slot_up = lax.all_to_all(send_wu, "dev", 0, 0, tiled=True).reshape(model_width, hidden_width)
    slot_down_t = lax.all_to_all(send_wd, "dev", 0, 0, tiled=True).reshape(model_width, hidden_width)

    match, named, target = routing(expert_ids, slot_plan, slot_count, round_total)
    q_ids = jnp.arange(row_slots, dtype=jnp.int32)
    chooser = (named[None, :, :] > 0) & (target[None, :, :] == q_ids[:, None, None])
    pick_rows = jnp.sum(chooser.astype(jnp.float32), axis=-1)
    pick_half = pick_rows.astype(jnp.bfloat16)
    gates_f = router_gates.astype(jnp.float32)
    rank_gate = jnp.sum(jnp.where(match, gates_f[:, :, None], 0.0), axis=1)
    gate_send = jnp.sum(jnp.where(chooser, rank_gate[None, :, :], 0.0), axis=(1, 2)).astype(jnp.bfloat16)

    x_send = jnp.dot(pick_half, tokens, preferred_element_type=jnp.float32).astype(jnp.bfloat16)
    dy_send = jnp.dot(pick_half, grad_out, preferred_element_type=jnp.float32).astype(jnp.bfloat16)
    got_x = lax.all_to_all(x_send.reshape(slot_count, CAP, model_width), "dev", 0, 0, tiled=True)
    got_dy = lax.all_to_all(dy_send.reshape(slot_count, CAP, model_width), "dev", 0, 0, tiled=True)
    got_gate = lax.all_to_all(gate_send.reshape(slot_count, CAP), "dev", 0, 0, tiled=True)
    x_rows = lax.all_gather(got_x.reshape(row_slots, model_width), "node", axis=0, tiled=True)
    dy_rows = lax.all_gather(got_dy.reshape(row_slots, model_width), "node", axis=0, tiled=True)
    gate_rows = lax.all_gather(got_gate.reshape(row_slots), "node", axis=0, tiled=True).astype(
        jnp.float32
    )[:, None]

    gate_pre = jnp.dot(x_rows, slot_gate, preferred_element_type=jnp.float32)
    up_pre = jnp.dot(x_rows, slot_up, preferred_element_type=jnp.float32)
    back_proj = jnp.dot(dy_rows, slot_down_t, preferred_element_type=jnp.float32)
    sigmoid_gate = jax.nn.sigmoid(gate_pre)
    active = gate_pre * sigmoid_gate
    hidden = active * up_pre
    scaled_back = gate_rows * back_proj
    d_gate = (scaled_back * up_pre * sigmoid_gate * (1.0 + gate_pre * (1.0 - sigmoid_gate))).astype(
        jnp.bfloat16
    )
    d_up = (scaled_back * active).astype(jnp.bfloat16)
    scaled_hidden = (gate_rows * hidden).astype(jnp.bfloat16)
    gate_terms = jnp.sum(back_proj * hidden, axis=-1)

    acc_gate = jnp.einsum("rd,rh->dh", x_rows, d_gate, preferred_element_type=jnp.float32)
    acc_up = jnp.einsum("rd,rh->dh", x_rows, d_up, preferred_element_type=jnp.float32)
    acc_down = jnp.einsum("rd,rh->dh", dy_rows, scaled_hidden, preferred_element_type=jnp.float32)
    row_terms = jnp.einsum("rh,dh->rd", d_gate, slot_gate, preferred_element_type=jnp.float32)
    row_terms = row_terms + jnp.einsum("rh,dh->rd", d_up, slot_up, preferred_element_type=jnp.float32)

    summed_rows = lax.psum_scatter(row_terms, "node", scatter_dimension=0, tiled=True)
    summed_gates = lax.psum_scatter(gate_terms, "node", scatter_dimension=0, tiled=True)
    back_rows = lax.all_to_all(summed_rows.reshape(slot_count, CAP, model_width), "dev", 0, 0, tiled=True)
    back_gates = lax.all_to_all(summed_gates.reshape(slot_count, CAP), "dev", 0, 0, tiled=True)

    grad_tokens = jnp.einsum(
        "qt,qd->td",
        pick_rows,
        back_rows.reshape(row_slots, model_width),
        precision=lax.Precision.HIGHEST,
    ).astype(jnp.bfloat16)
    back_q = back_gates.reshape(row_slots)
    rank_back = jnp.sum(jnp.where(chooser, back_q[:, None, None], 0.0), axis=0)
    grad_gates = jnp.sum(jnp.where(match, rank_back[:, None, :], 0.0), axis=-1)

    def pair_sum(acc):
        sent = acc.astype(jnp.bfloat16).reshape(slot_count, chunk, hidden_width)
        got = lax.all_to_all(sent, "dev", 0, 0, tiled=True)
        got = got.reshape(round_total, REPS, chunk, hidden_width).astype(jnp.float32)
        return jnp.sum(got, axis=1).astype(jnp.bfloat16)

    grad_w_gate = pair_sum(acc_gate)
    grad_w_up = pair_sum(acc_up)
    grad_w_down = jnp.swapaxes(pair_sum(acc_down), 1, 2)
    return (grad_tokens, grad_gates, grad_w_gate, grad_w_up, grad_w_down)


def solution(mesh):
    return jax.shard_map(
        local,
        mesh=mesh,
        in_specs=(
            P(("node", "dev"), None),
            P(("node", "dev"), None),
            P(("node", "dev"), None),
            P(("node", "dev"), None),
            P(),
            P(None, "dev", "node"),
            P(None, "dev", "node"),
            P(None, "node", "dev"),
        ),
        out_specs=(
            P(("node", "dev"), None),
            P(("node", "dev"), None),
            P(None, "dev", "node"),
            P(None, "dev", "node"),
            P(None, "node", "dev"),
        ),
        check_vma=False,
    )
```

```python
import jax
import jax.numpy as jnp
from jax import lax
from jax.sharding import PartitionSpec as P

TOP = 8
CAP = 2
REPS = 2
LANE = 128


def routing(expert_ids, slot_plan, slot_count, round_total):
    expert_count = slot_plan.shape[0]
    in_round = (slot_plan[:, 0] < slot_count).astype(jnp.int32)
    expert_rank = jnp.cumsum(in_round) - 1
    rank_match = (in_round[:, None] > 0) & (
        expert_rank[:, None] == jnp.arange(round_total, dtype=jnp.int32)[None, :]
    )
    hot_ids = jnp.sum(
        jnp.where(rank_match, jnp.arange(expert_count, dtype=jnp.int32)[:, None], 0), axis=0
    )
    match = expert_ids[:, :, None] == hot_ids[None, None, :]
    named = jnp.sum(match.astype(jnp.int32), axis=1)
    tok_rows = expert_ids.shape[0]
    earlier = (
        jnp.arange(tok_rows, dtype=jnp.int32)[None, :] < jnp.arange(tok_rows, dtype=jnp.int32)[:, None]
    ).astype(jnp.bfloat16)
    before = jnp.dot(earlier, named.astype(jnp.bfloat16), preferred_element_type=jnp.float32).astype(
        jnp.int32
    )
    per_rank = REPS * CAP
    target = per_rank * jnp.arange(round_total, dtype=jnp.int32)[None, :] + before
    return match, named, target


def local(tokens, grad_out, router_gates, expert_ids, slot_plan, w_gate, w_up, w_down):
    col_count = lax.axis_size("dev")
    node_count = lax.axis_size("node")
    tok_rows, model_width = tokens.shape
    round_total, chunk, node_hidden = w_gate.shape
    half = node_hidden // REPS
    per_rank = REPS * CAP
    row_slots = round_total * per_rank
    wide = model_width + LANE

    def split_cols(w):
        w = w.reshape(round_total, chunk, REPS, half)
        return jnp.swapaxes(w, 1, 2).reshape(col_count, chunk, half)

    send_wg = split_cols(w_gate)
    send_wu = split_cols(w_up)
    send_wd = split_cols(jnp.swapaxes(w_down, 1, 2))
    slot_gate = lax.all_to_all(send_wg, "dev", 0, 0, tiled=True).reshape(model_width, half)
    slot_up = lax.all_to_all(send_wu, "dev", 0, 0, tiled=True).reshape(model_width, half)
    slot_down_t = lax.all_to_all(send_wd, "dev", 0, 0, tiled=True).reshape(model_width, half)

    match, named, target = routing(expert_ids, slot_plan, col_count, round_total)
    q_ids = jnp.arange(row_slots, dtype=jnp.int32)
    chooser = (named[None, :, :] > 0) & (target[None, :, :] == q_ids[:, None, None])
    pick_rows = jnp.sum(chooser.astype(jnp.float32), axis=-1)
    pick_half = pick_rows.astype(jnp.bfloat16)
    gates_f = router_gates.astype(jnp.float32)
    rank_gate = jnp.sum(jnp.where(match, gates_f[:, :, None], 0.0), axis=1)
    gate_send = jnp.sum(jnp.where(chooser, rank_gate[None, :, :], 0.0), axis=(1, 2)).astype(jnp.bfloat16)

    x_send = jnp.dot(pick_half, tokens, preferred_element_type=jnp.float32).astype(jnp.bfloat16)
    dy_send = jnp.dot(pick_half, grad_out, preferred_element_type=jnp.float32).astype(jnp.bfloat16)
    gate_block = jnp.zeros((row_slots, LANE), jnp.bfloat16).at[:, 0].set(gate_send)
    dy_send = jnp.concatenate([dy_send, gate_block], axis=1)

    def to_cols(rows, width):
        rows = rows.reshape(round_total, 1, per_rank, width)
        rows = jnp.broadcast_to(rows, (round_total, REPS, per_rank, width))
        rows = rows.reshape(col_count, per_rank, width)
        got = lax.all_to_all(rows, "dev", 0, 0, tiled=True)
        return lax.all_gather(got.reshape(col_count * per_rank, width), "node", axis=0, tiled=True)

    x_rows = to_cols(x_send, model_width)
    dy_ext = to_cols(dy_send, wide)
    dy_rows = dy_ext[:, :model_width]
    gate_rows = dy_ext[:, model_width].astype(jnp.float32)[:, None]

    gate_pre = jnp.dot(x_rows, slot_gate, preferred_element_type=jnp.float32)
    up_pre = jnp.dot(x_rows, slot_up, preferred_element_type=jnp.float32)
    back_proj = jnp.dot(dy_rows, slot_down_t, preferred_element_type=jnp.float32)
    sigmoid_gate = jax.nn.sigmoid(gate_pre)
    active = gate_pre * sigmoid_gate
    hidden = active * up_pre
    scaled_back = gate_rows * back_proj
    d_gate = (scaled_back * up_pre * sigmoid_gate * (1.0 + gate_pre * (1.0 - sigmoid_gate))).astype(
        jnp.bfloat16
    )
    d_up = (scaled_back * active).astype(jnp.bfloat16)
    scaled_hidden = (gate_rows * hidden).astype(jnp.bfloat16)
    gate_terms = jnp.sum(back_proj * hidden, axis=-1)

    row_count = x_rows.shape[0]
    first_slot = (jnp.arange(row_count, dtype=jnp.int32) % REPS == 0)[:, None]

    def by_slot(d):
        zero = jnp.zeros((), d.dtype)
        return jnp.concatenate([jnp.where(first_slot, d, zero), jnp.where(first_slot, zero, d)], axis=1)

    def slot_pair_sum(rows, d):
        acc = jnp.einsum("rd,rh->dh", rows, by_slot(d), preferred_element_type=jnp.float32)
        acc = acc.astype(jnp.bfloat16).astype(jnp.float32)
        return (acc[:, :half] + acc[:, half:]).astype(jnp.bfloat16)

    grad_gate_cols = slot_pair_sum(x_rows, d_gate)
    grad_up_cols = slot_pair_sum(x_rows, d_up)
    grad_down_cols = slot_pair_sum(dy_rows, scaled_hidden)

    row_terms = jnp.einsum("rh,dh->rd", d_gate, slot_gate, preferred_element_type=jnp.float32)
    row_terms = row_terms + jnp.einsum("rh,dh->rd", d_up, slot_up, preferred_element_type=jnp.float32)
    term_block = jnp.zeros((row_count, LANE), jnp.float32).at[:, 0].set(gate_terms)
    row_ext = jnp.concatenate([row_terms, term_block], axis=1)

    summed = lax.psum_scatter(row_ext, "node", scatter_dimension=0, tiled=True)
    back = lax.all_to_all(summed.reshape(col_count, per_rank, wide), "dev", 0, 0, tiled=True)
    back = jnp.sum(back.reshape(round_total, REPS, per_rank, wide), axis=1).reshape(row_slots, wide)

    grad_tokens = jnp.einsum(
        "qt,qd->td",
        pick_rows,
        back[:, :model_width],
        precision=lax.Precision.HIGHEST,
    ).astype(jnp.bfloat16)
    back_q = back[:, model_width]
    rank_back = jnp.sum(jnp.where(chooser, back_q[:, None, None], 0.0), axis=0)
    grad_gates = jnp.sum(jnp.where(match, rank_back[:, None, :], 0.0), axis=-1)

    def home(cols):
        sent = cols.reshape(col_count, chunk, half)
        got = lax.all_to_all(sent, "dev", 0, 0, tiled=True)
        return jnp.swapaxes(got.reshape(round_total, REPS, chunk, half), 1, 2).reshape(
            round_total, chunk, node_hidden
        )

    grad_w_gate = home(grad_gate_cols)
    grad_w_up = home(grad_up_cols)
    grad_w_down = jnp.swapaxes(home(grad_down_cols), 1, 2)
    del node_count
    return (grad_tokens, grad_gates, grad_w_gate, grad_w_up, grad_w_down)


def solution(mesh):
    return jax.shard_map(
        local,
        mesh=mesh,
        in_specs=(
            P(("node", "dev"), None),
            P(("node", "dev"), None),
            P(("node", "dev"), None),
            P(("node", "dev"), None),
            P(),
            P(None, "dev", "node"),
            P(None, "dev", "node"),
            P(None, "node", "dev"),
        ),
        out_specs=(
            P(("node", "dev"), None),
            P(("node", "dev"), None),
            P(None, "dev", "node"),
            P(None, "dev", "node"),
            P(None, "node", "dev"),
        ),
        check_vma=False,
    )
```

```python
import jax
import jax.numpy as jnp
from jax import lax
from jax.sharding import PartitionSpec as P

TOP = 8
CAP = 2
REPS = 2
LANE = 128


def routing(expert_ids, slot_plan, slot_count, round_total):
    expert_count = slot_plan.shape[0]
    in_round = (slot_plan[:, 0] < slot_count).astype(jnp.int32)
    expert_rank = jnp.cumsum(in_round) - 1
    rank_match = (in_round[:, None] > 0) & (
        expert_rank[:, None] == jnp.arange(round_total, dtype=jnp.int32)[None, :]
    )
    hot_ids = jnp.sum(
        jnp.where(rank_match, jnp.arange(expert_count, dtype=jnp.int32)[:, None], 0), axis=0
    )
    match = expert_ids[:, :, None] == hot_ids[None, None, :]
    named = jnp.sum(match.astype(jnp.int32), axis=1)
    tok_rows = expert_ids.shape[0]
    earlier = (
        jnp.arange(tok_rows, dtype=jnp.int32)[None, :] < jnp.arange(tok_rows, dtype=jnp.int32)[:, None]
    ).astype(jnp.bfloat16)
    before = jnp.dot(earlier, named.astype(jnp.bfloat16), preferred_element_type=jnp.float32).astype(
        jnp.int32
    )
    per_rank = REPS * CAP
    target = per_rank * jnp.arange(round_total, dtype=jnp.int32)[None, :] + before
    return match, named, target


def local(tokens, grad_out, router_gates, expert_ids, slot_plan, w_gate, w_up, w_down):
    col_count = lax.axis_size("dev")
    node_count = lax.axis_size("node")
    tok_rows, model_width = tokens.shape
    round_total, chunk, node_hidden = w_gate.shape
    half = node_hidden // REPS
    per_rank = REPS * CAP
    row_slots = round_total * per_rank
    wide = model_width + LANE

    def split_cols(w):
        w = w.reshape(round_total, chunk, REPS, half)
        return jnp.swapaxes(w, 1, 2).reshape(col_count, chunk, half)

    send_wg = split_cols(w_gate)
    send_wu = split_cols(w_up)
    send_wd = split_cols(jnp.swapaxes(w_down, 1, 2))
    slot_gate = lax.all_to_all(send_wg, "dev", 0, 0, tiled=True).reshape(model_width, half)
    slot_up = lax.all_to_all(send_wu, "dev", 0, 0, tiled=True).reshape(model_width, half)
    slot_down_t = lax.all_to_all(send_wd, "dev", 0, 0, tiled=True).reshape(model_width, half)

    match, named, target = routing(expert_ids, slot_plan, col_count, round_total)
    q_ids = jnp.arange(row_slots, dtype=jnp.int32)
    chooser = (named[None, :, :] > 0) & (target[None, :, :] == q_ids[:, None, None])
    pick_rows = jnp.sum(chooser.astype(jnp.float32), axis=-1)
    pick_half = pick_rows.astype(jnp.bfloat16)
    gates_f = router_gates.astype(jnp.float32)
    rank_gate = jnp.sum(jnp.where(match, gates_f[:, :, None], 0.0), axis=1)
    gate_send = jnp.sum(jnp.where(chooser, rank_gate[None, :, :], 0.0), axis=(1, 2)).astype(jnp.bfloat16)

    x_send = jnp.dot(pick_half, tokens, preferred_element_type=jnp.float32).astype(jnp.bfloat16)
    dy_send = jnp.dot(pick_half, grad_out, preferred_element_type=jnp.float32).astype(jnp.bfloat16)
    gate_block = jnp.zeros((row_slots, LANE), jnp.bfloat16).at[:, 0].set(gate_send)
    dy_send = jnp.concatenate([dy_send, gate_block], axis=1)

    both_send = jnp.concatenate([x_send, dy_send], axis=1)
    both_width = model_width + wide
    both = both_send.reshape(round_total, 1, per_rank, both_width)
    both = jnp.broadcast_to(both, (round_total, REPS, per_rank, both_width))
    both = lax.all_to_all(both.reshape(col_count, per_rank, both_width), "dev", 0, 0, tiled=True)
    both = both.reshape(col_count * per_rank, both_width)
    x_rows = lax.all_gather(both[:, :model_width], "node", axis=0, tiled=True)
    dy_ext = lax.all_gather(both[:, model_width:], "node", axis=0, tiled=True)
    dy_rows = dy_ext[:, :model_width]
    gate_rows = dy_ext[:, model_width].astype(jnp.float32)[:, None]

    gate_pre = jnp.dot(x_rows, slot_gate, preferred_element_type=jnp.float32)
    up_pre = jnp.dot(x_rows, slot_up, preferred_element_type=jnp.float32)
    back_proj = jnp.dot(dy_rows, slot_down_t, preferred_element_type=jnp.float32)
    sigmoid_gate = jax.nn.sigmoid(gate_pre)
    active = gate_pre * sigmoid_gate
    hidden = active * up_pre
    scaled_back = gate_rows * back_proj
    d_gate = (scaled_back * up_pre * sigmoid_gate * (1.0 + gate_pre * (1.0 - sigmoid_gate))).astype(
        jnp.bfloat16
    )
    d_up = (scaled_back * active).astype(jnp.bfloat16)
    scaled_hidden = (gate_rows * hidden).astype(jnp.bfloat16)
    gate_terms = jnp.sum(back_proj * hidden, axis=-1)

    row_count = x_rows.shape[0]
    first_slot = (jnp.arange(row_count, dtype=jnp.int32) % REPS == 0)[:, None]

    def by_slot(d):
        zero = jnp.zeros((), d.dtype)
        return jnp.concatenate([jnp.where(first_slot, d, zero), jnp.where(first_slot, zero, d)], axis=1)

    def slot_pair_sum(rows, d):
        acc = jnp.einsum("rd,rh->dh", rows, by_slot(d), preferred_element_type=jnp.float32)
        acc = lax.reduce_precision(acc, exponent_bits=8, mantissa_bits=7)
        return (acc[:, :half] + acc[:, half:]).astype(jnp.bfloat16)

    grad_gate_cols = slot_pair_sum(x_rows, d_gate)
    grad_up_cols = slot_pair_sum(x_rows, d_up)
    grad_down_cols = slot_pair_sum(dy_rows, scaled_hidden)

    pad_rows = ((0, LANE), (0, 0))
    row_ext = jnp.einsum("rh,dh->rd", d_gate, jnp.pad(slot_gate, pad_rows), preferred_element_type=jnp.float32)
    row_ext = row_ext + jnp.einsum(
        "rh,dh->rd", d_up, jnp.pad(slot_up, pad_rows), preferred_element_type=jnp.float32
    )
    term_col = jnp.arange(wide, dtype=jnp.int32)[None, :] == model_width
    row_ext = row_ext + jnp.where(term_col, gate_terms[:, None], 0.0)

    summed = lax.psum_scatter(row_ext, "node", scatter_dimension=0, tiled=True)
    back = lax.all_to_all(summed.reshape(col_count, per_rank, wide), "dev", 0, 0, tiled=True)
    back = jnp.sum(back.reshape(round_total, REPS, per_rank, wide), axis=1).reshape(row_slots, wide)

    grad_tokens = jnp.einsum(
        "qt,qd->td",
        pick_rows,
        back[:, :model_width],
        precision=lax.Precision.HIGHEST,
    ).astype(jnp.bfloat16)
    back_q = back[:, model_width]
    rank_back = jnp.sum(jnp.where(chooser, back_q[:, None, None], 0.0), axis=0)
    grad_gates = jnp.sum(jnp.where(match, rank_back[:, None, :], 0.0), axis=-1)

    def home(cols):
        sent = cols.reshape(col_count, chunk, half)
        got = lax.all_to_all(sent, "dev", 0, 0, tiled=True).reshape(round_total, REPS, chunk, half)
        return jnp.concatenate([got[:, h] for h in range(REPS)], axis=-1)

    grad_w_gate = home(grad_gate_cols)
    grad_w_up = home(grad_up_cols)
    got_down = lax.all_to_all(grad_down_cols.reshape(col_count, chunk, half), "dev", 0, 0, tiled=True)
    got_down = got_down.reshape(round_total, REPS, chunk, half)
    grad_w_down = jnp.concatenate([jnp.swapaxes(got_down[:, h], 1, 2) for h in range(REPS)], axis=1)
    del node_count
    return (grad_tokens, grad_gates, grad_w_gate, grad_w_up, grad_w_down)


def solution(mesh):
    return jax.shard_map(
        local,
        mesh=mesh,
        in_specs=(
            P(("node", "dev"), None),
            P(("node", "dev"), None),
            P(("node", "dev"), None),
            P(("node", "dev"), None),
            P(),
            P(None, "dev", "node"),
            P(None, "dev", "node"),
            P(None, "node", "dev"),
        ),
        out_specs=(
            P(("node", "dev"), None),
            P(("node", "dev"), None),
            P(None, "dev", "node"),
            P(None, "dev", "node"),
            P(None, "node", "dev"),
        ),
        check_vma=False,
    )
```

```python
import jax
import jax.numpy as jnp
from jax import lax
from jax.sharding import PartitionSpec as P

TOP = 8
CAP = 2
REPS = 2
LANE = 128


def routing(expert_ids, slot_plan, slot_count, round_total):
    expert_count = slot_plan.shape[0]
    in_round = (slot_plan[:, 0] < slot_count).astype(jnp.int32)
    expert_rank = jnp.cumsum(in_round) - 1
    rank_match = (in_round[:, None] > 0) & (
        expert_rank[:, None] == jnp.arange(round_total, dtype=jnp.int32)[None, :]
    )
    hot_ids = jnp.sum(
        jnp.where(rank_match, jnp.arange(expert_count, dtype=jnp.int32)[:, None], 0), axis=0
    )
    match = expert_ids[:, :, None] == hot_ids[None, None, :]
    named = jnp.sum(match.astype(jnp.int32), axis=1)
    tok_rows = expert_ids.shape[0]
    earlier = (
        jnp.arange(tok_rows, dtype=jnp.int32)[None, :] < jnp.arange(tok_rows, dtype=jnp.int32)[:, None]
    ).astype(jnp.bfloat16)
    before = jnp.dot(earlier, named.astype(jnp.bfloat16), preferred_element_type=jnp.float32).astype(
        jnp.int32
    )
    per_rank = REPS * CAP
    target = per_rank * jnp.arange(round_total, dtype=jnp.int32)[None, :] + before
    return match, named, target


def local(tokens, grad_out, router_gates, expert_ids, slot_plan, w_gate, w_up, w_down):
    col_count = lax.axis_size("dev")
    node_count = lax.axis_size("node")
    tok_rows, model_width = tokens.shape
    round_total, chunk, node_hidden = w_gate.shape
    half = node_hidden // REPS
    per_rank = REPS * CAP
    row_slots = round_total * per_rank
    wide = model_width + LANE

    def split_cols(w):
        w = w.reshape(round_total, chunk, REPS, half)
        return jnp.swapaxes(w, 1, 2).reshape(col_count, chunk, half)

    send_w = jnp.concatenate(
        [split_cols(w_gate), split_cols(w_up), split_cols(jnp.swapaxes(w_down, 1, 2))], axis=1
    )
    got_w = lax.all_to_all(send_w, "dev", 0, 0, tiled=True).reshape(col_count, 3, chunk, half)
    slot_gate = got_w[:, 0].reshape(model_width, half)
    slot_up = got_w[:, 1].reshape(model_width, half)
    slot_down_t = got_w[:, 2].reshape(model_width, half)

    match, named, target = routing(expert_ids, slot_plan, col_count, round_total)
    q_ids = jnp.arange(row_slots, dtype=jnp.int32)
    chooser = (named[None, :, :] > 0) & (target[None, :, :] == q_ids[:, None, None])
    pick_rows = jnp.sum(chooser.astype(jnp.float32), axis=-1)
    pick_half = pick_rows.astype(jnp.bfloat16)
    gates_f = router_gates.astype(jnp.float32)
    rank_gate = jnp.sum(jnp.where(match, gates_f[:, :, None], 0.0), axis=1)
    gate_send = jnp.sum(jnp.where(chooser, rank_gate[None, :, :], 0.0), axis=(1, 2)).astype(jnp.bfloat16)

    x_send = jnp.dot(pick_half, tokens, preferred_element_type=jnp.float32).astype(jnp.bfloat16)
    dy_send = jnp.dot(pick_half, grad_out, preferred_element_type=jnp.float32).astype(jnp.bfloat16)
    gate_block = jnp.zeros((row_slots, LANE), jnp.bfloat16).at[:, 0].set(gate_send)
    dy_send = jnp.concatenate([dy_send, gate_block], axis=1)

    both_send = jnp.concatenate([x_send, dy_send], axis=1)
    both_width = model_width + wide
    both = both_send.reshape(round_total, 1, per_rank, both_width)
    both = jnp.broadcast_to(both, (round_total, REPS, per_rank, both_width))
    both = lax.all_to_all(both.reshape(col_count, per_rank, both_width), "dev", 0, 0, tiled=True)
    both = both.reshape(col_count * per_rank, both_width)
    x_rows = lax.all_gather(both[:, :model_width], "node", axis=0, tiled=True)
    dy_ext = lax.all_gather(both[:, model_width:], "node", axis=0, tiled=True)
    dy_rows = dy_ext[:, :model_width]
    gate_rows = dy_ext[:, model_width].astype(jnp.float32)[:, None]

    gate_pre = jnp.dot(x_rows, slot_gate, preferred_element_type=jnp.float32)
    up_pre = jnp.dot(x_rows, slot_up, preferred_element_type=jnp.float32)
    back_proj = jnp.dot(dy_rows, slot_down_t, preferred_element_type=jnp.float32)
    sigmoid_gate = jax.nn.sigmoid(gate_pre)
    active = gate_pre * sigmoid_gate
    hidden = active * up_pre
    scaled_back = gate_rows * back_proj
    d_gate = (scaled_back * up_pre * sigmoid_gate * (1.0 + gate_pre * (1.0 - sigmoid_gate))).astype(
        jnp.bfloat16
    )
    d_up = (scaled_back * active).astype(jnp.bfloat16)
    scaled_hidden = (gate_rows * hidden).astype(jnp.bfloat16)
    gate_terms = jnp.sum(back_proj * hidden, axis=-1)

    row_count = x_rows.shape[0]
    first_slot = (jnp.arange(row_count, dtype=jnp.int32) % REPS == 0)[:, None]

    def by_slot(d):
        zero = jnp.zeros((), d.dtype)
        return jnp.concatenate([jnp.where(first_slot, d, zero), jnp.where(first_slot, zero, d)], axis=1)

    def slot_pair_sum(rows, d):
        acc = jnp.einsum("rd,rh->dh", rows, by_slot(d), preferred_element_type=jnp.float32)
        acc = lax.reduce_precision(acc, exponent_bits=8, mantissa_bits=7)
        return (acc[:, :half] + acc[:, half:]).astype(jnp.bfloat16)

    grad_gate_cols = slot_pair_sum(x_rows, d_gate)
    grad_up_cols = slot_pair_sum(x_rows, d_up)
    grad_down_cols = slot_pair_sum(dy_rows, scaled_hidden)

    pad_rows = ((0, LANE), (0, 0))
    row_ext = jnp.einsum("rh,dh->rd", d_gate, jnp.pad(slot_gate, pad_rows), preferred_element_type=jnp.float32)
    row_ext = row_ext + jnp.einsum(
        "rh,dh->rd", d_up, jnp.pad(slot_up, pad_rows), preferred_element_type=jnp.float32
    )
    term_col = jnp.arange(wide, dtype=jnp.int32)[None, :] == model_width
    row_ext = row_ext + jnp.where(term_col, gate_terms[:, None], 0.0)

    summed = lax.psum_scatter(row_ext, "node", scatter_dimension=0, tiled=True)
    back = lax.all_to_all(summed.reshape(col_count, per_rank, wide), "dev", 0, 0, tiled=True)
    back = jnp.sum(back.reshape(round_total, REPS, per_rank, wide), axis=1).reshape(row_slots, wide)

    grad_tokens = jnp.einsum(
        "qt,qd->td",
        pick_rows,
        back[:, :model_width],
        precision=lax.Precision.HIGH,
    ).astype(jnp.bfloat16)
    back_q = back[:, model_width]
    rank_back = jnp.sum(jnp.where(chooser, back_q[:, None, None], 0.0), axis=0)
    grad_gates = jnp.sum(jnp.where(match, rank_back[:, None, :], 0.0), axis=-1)

    cols = jnp.concatenate(
        [c.reshape(col_count, chunk, half) for c in (grad_gate_cols, grad_up_cols, grad_down_cols)], axis=1
    )
    got = lax.all_to_all(cols, "dev", 0, 0, tiled=True).reshape(round_total, REPS, 3, chunk, half)
    grad_w_gate = jnp.concatenate([got[:, h, 0] for h in range(REPS)], axis=-1)
    grad_w_up = jnp.concatenate([got[:, h, 1] for h in range(REPS)], axis=-1)
    grad_w_down = jnp.concatenate([jnp.swapaxes(got[:, h, 2], 1, 2) for h in range(REPS)], axis=1)
    del node_count
    return (grad_tokens, grad_gates, grad_w_gate, grad_w_up, grad_w_down)


def solution(mesh):
    return jax.shard_map(
        local,
        mesh=mesh,
        in_specs=(
            P(("node", "dev"), None),
            P(("node", "dev"), None),
            P(("node", "dev"), None),
            P(("node", "dev"), None),
            P(),
            P(None, "dev", "node"),
            P(None, "dev", "node"),
            P(None, "node", "dev"),
        ),
        out_specs=(
            P(("node", "dev"), None),
            P(("node", "dev"), None),
            P(None, "dev", "node"),
            P(None, "dev", "node"),
            P(None, "node", "dev"),
        ),
        check_vma=False,
    )
```

```python
import jax
import jax.numpy as jnp
from jax import lax
from jax.sharding import PartitionSpec as P

TOP = 8
CAP = 2
REPS = 2
LANE = 128


def routing(expert_ids, slot_plan, slot_count, round_total):
    expert_count = slot_plan.shape[0]
    in_round = (slot_plan[:, 0] < slot_count).astype(jnp.int32)
    expert_rank = jnp.cumsum(in_round) - 1
    rank_match = (in_round[:, None] > 0) & (
        expert_rank[:, None] == jnp.arange(round_total, dtype=jnp.int32)[None, :]
    )
    hot_ids = jnp.sum(
        jnp.where(rank_match, jnp.arange(expert_count, dtype=jnp.int32)[:, None], 0), axis=0
    )
    match = expert_ids[:, :, None] == hot_ids[None, None, :]
    named = jnp.sum(match.astype(jnp.int32), axis=1)
    tok_rows = expert_ids.shape[0]
    earlier = (
        jnp.arange(tok_rows, dtype=jnp.int32)[None, :] < jnp.arange(tok_rows, dtype=jnp.int32)[:, None]
    ).astype(jnp.bfloat16)
    before = jnp.dot(earlier, named.astype(jnp.bfloat16), preferred_element_type=jnp.float32).astype(
        jnp.int32
    )
    per_rank = REPS * CAP
    target = per_rank * jnp.arange(round_total, dtype=jnp.int32)[None, :] + before
    return match, named, target


def local(tokens, grad_out, router_gates, expert_ids, slot_plan, w_gate, w_up, w_down):
    col_count = lax.axis_size("dev")
    node_count = lax.axis_size("node")
    tok_rows, model_width = tokens.shape
    round_total, chunk, node_hidden = w_gate.shape
    half = node_hidden // REPS
    per_rank = REPS * CAP
    row_slots = round_total * per_rank
    wide = model_width + LANE

    stacked = jnp.stack([w_gate, w_up, jnp.swapaxes(w_down, 1, 2)], axis=2)
    stacked = stacked.reshape(round_total, chunk, 3, REPS, half).transpose(0, 3, 1, 2, 4)
    send_w = stacked.reshape(col_count, chunk, 3 * half)
    got_w = lax.all_to_all(send_w, "dev", 0, 0, tiled=True).reshape(model_width, 3 * half)
    slot_gate_up = got_w[:, : 2 * half]
    slot_down_t = got_w[:, 2 * half :]

    match, named, target = routing(expert_ids, slot_plan, col_count, round_total)
    q_ids = jnp.arange(row_slots, dtype=jnp.int32)
    chooser = (named[None, :, :] > 0) & (target[None, :, :] == q_ids[:, None, None])
    pick_rows = jnp.sum(chooser.astype(jnp.float32), axis=-1)
    pick_half = pick_rows.astype(jnp.bfloat16)
    gates_f = router_gates.astype(jnp.float32)
    rank_gate = jnp.sum(jnp.where(match, gates_f[:, :, None], 0.0), axis=1)
    gate_send = jnp.sum(jnp.where(chooser, rank_gate[None, :, :], 0.0), axis=(1, 2)).astype(jnp.bfloat16)

    x_send = jnp.dot(pick_half, tokens, preferred_element_type=jnp.float32).astype(jnp.bfloat16)
    dy_send = jnp.dot(pick_half, grad_out, preferred_element_type=jnp.float32).astype(jnp.bfloat16)
    gate_block = jnp.zeros((row_slots, LANE), jnp.bfloat16).at[:, 0].set(gate_send)
    dy_send = jnp.concatenate([dy_send, gate_block], axis=1)

    both_send = jnp.concatenate([x_send, dy_send], axis=1)
    both_width = model_width + wide
    both = both_send.reshape(round_total, 1, per_rank, both_width)
    both = jnp.broadcast_to(both, (round_total, REPS, per_rank, both_width))
    both = lax.all_to_all(both.reshape(col_count, per_rank, both_width), "dev", 0, 0, tiled=True)
    both = both.reshape(col_count * per_rank, both_width)
    x_rows = lax.all_gather(both[:, :model_width], "node", axis=0, tiled=True)
    dy_ext = lax.all_gather(both[:, model_width:], "node", axis=0, tiled=True)
    dy_rows = dy_ext[:, :model_width]
    gate_rows = dy_ext[:, model_width].astype(jnp.float32)[:, None]

    gate_up = jnp.dot(x_rows, slot_gate_up, preferred_element_type=jnp.float32)
    gate_pre = gate_up[:, :half]
    up_pre = gate_up[:, half:]
    back_proj = jnp.dot(dy_rows, slot_down_t, preferred_element_type=jnp.float32)
    sigmoid_gate = jax.nn.sigmoid(gate_pre)
    active = gate_pre * sigmoid_gate
    hidden = active * up_pre
    scaled_back = gate_rows * back_proj
    d_gate = (scaled_back * up_pre * sigmoid_gate * (1.0 + gate_pre * (1.0 - sigmoid_gate))).astype(
        jnp.bfloat16
    )
    d_up = (scaled_back * active).astype(jnp.bfloat16)
    scaled_hidden = (gate_rows * hidden).astype(jnp.bfloat16)
    gate_terms = jnp.sum(back_proj * hidden, axis=-1)

    row_count = x_rows.shape[0]
    first_slot = (jnp.arange(row_count, dtype=jnp.int32) % REPS == 0)[:, None]

    def by_slot(d):
        zero = jnp.zeros((), d.dtype)
        return jnp.concatenate([jnp.where(first_slot, d, zero), jnp.where(first_slot, zero, d)], axis=1)

    def pair_sum(acc):
        acc = lax.reduce_precision(acc, exponent_bits=8, mantissa_bits=7)
        return (acc[:, :half] + acc[:, half:]).astype(jnp.bfloat16)

    acc_gu = jnp.einsum(
        "rd,rh->dh", x_rows, jnp.concatenate([by_slot(d_gate), by_slot(d_up)], axis=1),
        preferred_element_type=jnp.float32,
    )
    grad_gate_cols = pair_sum(acc_gu[:, : 2 * half])
    grad_up_cols = pair_sum(acc_gu[:, 2 * half :])
    acc_down = jnp.einsum("rd,rh->dh", dy_rows, by_slot(scaled_hidden), preferred_element_type=jnp.float32)
    grad_down_cols = pair_sum(acc_down)

    d_both = jnp.concatenate([d_gate, d_up], axis=1)
    pad_rows = ((0, LANE), (0, 0))
    row_ext = jnp.einsum("rh,dh->rd", d_both, jnp.pad(slot_gate_up, pad_rows), preferred_element_type=jnp.float32)
    term_col = jnp.arange(wide, dtype=jnp.int32)[None, :] == model_width
    row_ext = row_ext + jnp.where(term_col, gate_terms[:, None], 0.0)

    summed = lax.psum_scatter(row_ext, "node", scatter_dimension=0, tiled=True)
    back = lax.all_to_all(summed.reshape(col_count, per_rank, wide), "dev", 0, 0, tiled=True)
    back = jnp.sum(back.reshape(round_total, REPS, per_rank, wide), axis=1).reshape(row_slots, wide)

    grad_tokens = jnp.einsum(
        "qt,qd->td",
        pick_rows,
        back[:, :model_width],
        precision=lax.Precision.HIGH,
    ).astype(jnp.bfloat16)
    back_q = back[:, model_width]
    rank_back = jnp.sum(jnp.where(chooser, back_q[:, None, None], 0.0), axis=0)
    grad_gates = jnp.sum(jnp.where(match, rank_back[:, None, :], 0.0), axis=-1)

    def home(cols):
        sent = cols.reshape(col_count, chunk, half)
        got = lax.all_to_all(sent, "dev", 0, 0, tiled=True).reshape(round_total, REPS, chunk, half)
        return jnp.concatenate([got[:, h] for h in range(REPS)], axis=-1)

    grad_w_gate = home(grad_gate_cols)
    grad_w_up = home(grad_up_cols)
    got_down = lax.all_to_all(grad_down_cols.reshape(col_count, chunk, half), "dev", 0, 0, tiled=True)
    got_down = got_down.reshape(round_total, REPS, chunk, half)
    grad_w_down = jnp.concatenate([jnp.swapaxes(got_down[:, h], 1, 2) for h in range(REPS)], axis=1)
    del node_count
    return (grad_tokens, grad_gates, grad_w_gate, grad_w_up, grad_w_down)


def solution(mesh):
    return jax.shard_map(
        local,
        mesh=mesh,
        in_specs=(
            P(("node", "dev"), None),
            P(("node", "dev"), None),
            P(("node", "dev"), None),
            P(("node", "dev"), None),
            P(),
            P(None, "dev", "node"),
            P(None, "dev", "node"),
            P(None, "node", "dev"),
        ),
        out_specs=(
            P(("node", "dev"), None),
            P(("node", "dev"), None),
            P(None, "dev", "node"),
            P(None, "dev", "node"),
            P(None, "node", "dev"),
        ),
        check_vma=False,
    )
```

```python
import jax
import jax.numpy as jnp
from jax import lax
from jax.sharding import PartitionSpec as P

TOP = 8
CAP = 2
REPS = 2
LANE = 128


def routing(expert_ids, slot_plan, slot_count, round_total):
    expert_count = slot_plan.shape[0]
    in_round = (slot_plan[:, 0] < slot_count).astype(jnp.int32)
    expert_rank = jnp.cumsum(in_round) - 1
    rank_match = (in_round[:, None] > 0) & (
        expert_rank[:, None] == jnp.arange(round_total, dtype=jnp.int32)[None, :]
    )
    hot_ids = jnp.sum(
        jnp.where(rank_match, jnp.arange(expert_count, dtype=jnp.int32)[:, None], 0), axis=0
    )
    match = expert_ids[:, :, None] == hot_ids[None, None, :]
    named = jnp.sum(match.astype(jnp.int32), axis=1)
    tok_rows = expert_ids.shape[0]
    earlier = (
        jnp.arange(tok_rows, dtype=jnp.int32)[None, :] < jnp.arange(tok_rows, dtype=jnp.int32)[:, None]
    ).astype(jnp.bfloat16)
    before = jnp.dot(earlier, named.astype(jnp.bfloat16), preferred_element_type=jnp.float32).astype(
        jnp.int32
    )
    per_rank = REPS * CAP
    target = per_rank * jnp.arange(round_total, dtype=jnp.int32)[None, :] + before
    return match, named, target


def local(tokens, grad_out, router_gates, expert_ids, slot_plan, w_gate, w_up, w_down):
    col_count = lax.axis_size("dev")
    node_count = lax.axis_size("node")
    tok_rows, model_width = tokens.shape
    round_total, chunk, node_hidden = w_gate.shape
    half = node_hidden // REPS
    per_rank = REPS * CAP
    row_slots = round_total * per_rank
    wide = model_width + LANE

    def split_cols(w):
        w = w.reshape(round_total, chunk, REPS, half)
        return jnp.swapaxes(w, 1, 2).reshape(col_count, chunk, half)

    send_wg = split_cols(w_gate)
    send_wu = split_cols(w_up)
    send_wd = split_cols(jnp.swapaxes(w_down, 1, 2))
    slot_gate = lax.all_to_all(send_wg, "dev", 0, 0, tiled=True).reshape(model_width, half)
    slot_up = lax.all_to_all(send_wu, "dev", 0, 0, tiled=True).reshape(model_width, half)
    slot_down_t = lax.all_to_all(send_wd, "dev", 0, 0, tiled=True).reshape(model_width, half)

    match, named, target = routing(expert_ids, slot_plan, col_count, round_total)
    q_ids = jnp.arange(row_slots, dtype=jnp.int32)
    chooser = (named[None, :, :] > 0) & (target[None, :, :] == q_ids[:, None, None])
    pick_rows = jnp.sum(chooser.astype(jnp.float32), axis=-1)
    pick_half = pick_rows.astype(jnp.bfloat16)
    gates_f = router_gates.astype(jnp.float32)
    rank_gate = jnp.sum(jnp.where(match, gates_f[:, :, None], 0.0), axis=1)
    gate_send = jnp.sum(jnp.where(chooser, rank_gate[None, :, :], 0.0), axis=(1, 2)).astype(jnp.bfloat16)

    x_send = jnp.dot(pick_half, tokens, preferred_element_type=jnp.float32).astype(jnp.bfloat16)
    dy_send = jnp.dot(pick_half, grad_out, preferred_element_type=jnp.float32).astype(jnp.bfloat16)
    gate_block = jnp.zeros((row_slots, LANE), jnp.bfloat16).at[:, 0].set(gate_send)
    dy_send = jnp.concatenate([dy_send, gate_block], axis=1)

    both_send = jnp.concatenate([x_send, dy_send], axis=1)
    both_width = model_width + wide
    both = both_send.reshape(round_total, 1, per_rank, both_width)
    both = jnp.broadcast_to(both, (round_total, REPS, per_rank, both_width))
    both = lax.all_to_all(both.reshape(col_count, per_rank, both_width), "dev", 0, 0, tiled=True)
    both = both.reshape(col_count * per_rank, both_width)
    x_rows = lax.all_gather(both[:, :model_width], "node", axis=0, tiled=True)
    dy_ext = lax.all_gather(both[:, model_width:], "node", axis=0, tiled=True)
    dy_rows = dy_ext[:, :model_width]
    gate_rows = dy_ext[:, model_width].astype(jnp.float32)[:, None]

    gate_pre = jnp.dot(x_rows, slot_gate, preferred_element_type=jnp.float32)
    up_pre = jnp.dot(x_rows, slot_up, preferred_element_type=jnp.float32)
    back_proj = jnp.dot(dy_rows, slot_down_t, preferred_element_type=jnp.float32)
    sigmoid_gate = jax.nn.sigmoid(gate_pre)
    active = gate_pre * sigmoid_gate
    hidden = active * up_pre
    scaled_back = gate_rows * back_proj
    d_gate = (scaled_back * up_pre * sigmoid_gate * (1.0 + gate_pre * (1.0 - sigmoid_gate))).astype(
        jnp.bfloat16
    )
    d_up = (scaled_back * active).astype(jnp.bfloat16)
    scaled_hidden = (gate_rows * hidden).astype(jnp.bfloat16)
    gate_terms = jnp.sum(back_proj * hidden, axis=-1)

    row_count = x_rows.shape[0]
    first_slot = (jnp.arange(row_count, dtype=jnp.int32) % REPS == 0)[:, None]

    def by_slot(d):
        zero = jnp.zeros((), d.dtype)
        return jnp.concatenate([jnp.where(first_slot, d, zero), jnp.where(first_slot, zero, d)], axis=1)

    def slot_pair_sum(rows, d):
        acc = jnp.einsum("rd,rh->dh", rows, by_slot(d), preferred_element_type=jnp.float32)
        acc = lax.reduce_precision(acc, exponent_bits=8, mantissa_bits=7)
        return (acc[:, :half] + acc[:, half:]).astype(jnp.bfloat16)

    grad_gate_cols = slot_pair_sum(x_rows, d_gate)
    grad_up_cols = slot_pair_sum(x_rows, d_up)
    grad_down_cols = slot_pair_sum(dy_rows, scaled_hidden)

    pad_rows = ((0, LANE), (0, 0))
    row_ext = jnp.einsum("rh,dh->rd", d_gate, jnp.pad(slot_gate, pad_rows), preferred_element_type=jnp.float32)
    row_ext = row_ext + jnp.einsum(
        "rh,dh->rd", d_up, jnp.pad(slot_up, pad_rows), preferred_element_type=jnp.float32
    )
    term_col = jnp.arange(wide, dtype=jnp.int32)[None, :] == model_width
    row_ext = row_ext + jnp.where(term_col, gate_terms[:, None], 0.0)

    summed = lax.psum_scatter(row_ext, "node", scatter_dimension=0, tiled=True)
    back = lax.all_to_all(summed.reshape(col_count, per_rank, wide), "dev", 0, 0, tiled=True)
    back = jnp.sum(back.reshape(round_total, REPS, per_rank, wide), axis=1).reshape(row_slots, wide)

    grad_tokens = jnp.einsum(
        "qt,qd->td",
        pick_rows,
        back[:, :model_width],
        precision=lax.Precision.HIGH,
    ).astype(jnp.bfloat16)
    back_q = back[:, model_width]
    rank_back = jnp.sum(jnp.where(chooser, back_q[:, None, None], 0.0), axis=0)
    grad_gates = jnp.sum(jnp.where(match, rank_back[:, None, :], 0.0), axis=-1)

    def home(cols):
        sent = cols.reshape(col_count, chunk, half)
        got = lax.all_to_all(sent, "dev", 0, 0, tiled=True).reshape(round_total, REPS, chunk, half)
        return jnp.concatenate([got[:, h] for h in range(REPS)], axis=-1)

    grad_w_gate = home(grad_gate_cols)
    grad_w_up = home(grad_up_cols)
    got_down = lax.all_to_all(grad_down_cols.reshape(col_count, chunk, half), "dev", 0, 0, tiled=True)
    got_down = got_down.reshape(round_total, REPS, chunk, half)
    grad_w_down = jnp.concatenate([jnp.swapaxes(got_down[:, h], 1, 2) for h in range(REPS)], axis=1)
    del node_count
    return (grad_tokens, grad_gates, grad_w_gate, grad_w_up, grad_w_down)


def solution(mesh):
    return jax.shard_map(
        local,
        mesh=mesh,
        in_specs=(
            P(("node", "dev"), None),
            P(("node", "dev"), None),
            P(("node", "dev"), None),
            P(("node", "dev"), None),
            P(),
            P(None, "dev", "node"),
            P(None, "dev", "node"),
            P(None, "node", "dev"),
        ),
        out_specs=(
            P(("node", "dev"), None),
            P(("node", "dev"), None),
            P(None, "dev", "node"),
            P(None, "dev", "node"),
            P(None, "node", "dev"),
        ),
        check_vma=False,
    )
```

```python
import jax
import jax.numpy as jnp
from jax import lax
from jax.sharding import PartitionSpec as P

TOP = 8
CAP = 2
REPS = 2
LANE = 128


def routing(expert_ids, slot_plan, slot_count, round_total):
    expert_count = slot_plan.shape[0]
    in_round = (slot_plan[:, 0] < slot_count).astype(jnp.int32)
    expert_rank = jnp.cumsum(in_round) - 1
    rank_match = (in_round[:, None] > 0) & (
        expert_rank[:, None] == jnp.arange(round_total, dtype=jnp.int32)[None, :]
    )
    hot_ids = jnp.sum(
        jnp.where(rank_match, jnp.arange(expert_count, dtype=jnp.int32)[:, None], 0), axis=0
    )
    match = expert_ids[:, :, None] == hot_ids[None, None, :]
    named = jnp.sum(match.astype(jnp.int32), axis=1)
    tok_rows = expert_ids.shape[0]
    earlier = (
        jnp.arange(tok_rows, dtype=jnp.int32)[None, :] < jnp.arange(tok_rows, dtype=jnp.int32)[:, None]
    ).astype(jnp.bfloat16)
    before = jnp.dot(earlier, named.astype(jnp.bfloat16), preferred_element_type=jnp.float32).astype(
        jnp.int32
    )
    per_rank = REPS * CAP
    target = per_rank * jnp.arange(round_total, dtype=jnp.int32)[None, :] + before
    return match, named, target


def local(tokens, grad_out, router_gates, expert_ids, slot_plan, w_gate, w_up, w_down):
    col_count = lax.axis_size("dev")
    node_count = lax.axis_size("node")
    tok_rows, model_width = tokens.shape
    round_total, chunk, node_hidden = w_gate.shape
    half = node_hidden // REPS
    per_rank = REPS * CAP
    row_slots = round_total * per_rank
    wide = model_width + LANE

    def split_cols(w):
        w = w.reshape(round_total, chunk, REPS, half)
        return jnp.swapaxes(w, 1, 2).reshape(col_count, chunk, half)

    send_wg = split_cols(w_gate)
    send_wu = split_cols(w_up)
    send_wd = split_cols(jnp.swapaxes(w_down, 1, 2))
    slot_gate = lax.all_to_all(send_wg, "dev", 0, 0, tiled=True).reshape(model_width, half)
    slot_up = lax.all_to_all(send_wu, "dev", 0, 0, tiled=True).reshape(model_width, half)
    slot_down_t = lax.all_to_all(send_wd, "dev", 0, 0, tiled=True).reshape(model_width, half)

    match, named, target = routing(expert_ids, slot_plan, col_count, round_total)
    q_ids = jnp.arange(row_slots, dtype=jnp.int32)
    chooser = (named[None, :, :] > 0) & (target[None, :, :] == q_ids[:, None, None])
    pick_rows = jnp.sum(chooser.astype(jnp.float32), axis=-1)
    pick_half = pick_rows.astype(jnp.bfloat16)
    gates_f = router_gates.astype(jnp.float32)
    rank_gate = jnp.sum(jnp.where(match, gates_f[:, :, None], 0.0), axis=1)
    gate_send = jnp.sum(jnp.where(chooser, rank_gate[None, :, :], 0.0), axis=(1, 2)).astype(jnp.bfloat16)

    x_send = jnp.dot(pick_half, tokens, preferred_element_type=jnp.float32).astype(jnp.bfloat16)
    dy_send = jnp.dot(pick_half, grad_out, preferred_element_type=jnp.float32).astype(jnp.bfloat16)
    gate_block = jnp.zeros((row_slots, LANE), jnp.bfloat16).at[:, 0].set(gate_send)
    dy_send = jnp.concatenate([dy_send, gate_block], axis=1)

    both_send = jnp.concatenate([x_send, dy_send], axis=1)
    both_width = model_width + wide
    both = both_send.reshape(round_total, 1, per_rank, both_width)
    both = jnp.broadcast_to(both, (round_total, REPS, per_rank, both_width))
    flat = per_rank * both_width // LANE
    both = lax.all_to_all(both.reshape(col_count, flat, LANE), "dev", 0, 0, tiled=True)
    both = both.reshape(col_count * per_rank, both_width)
    x_rows = lax.all_gather(both[:, :model_width], "node", axis=0, tiled=True)
    dy_ext = lax.all_gather(both[:, model_width:], "node", axis=0, tiled=True)
    dy_rows = dy_ext[:, :model_width]
    gate_rows = dy_ext[:, model_width].astype(jnp.float32)[:, None]

    gate_pre = jnp.dot(x_rows, slot_gate, preferred_element_type=jnp.float32)
    up_pre = jnp.dot(x_rows, slot_up, preferred_element_type=jnp.float32)
    back_proj = jnp.dot(dy_rows, slot_down_t, preferred_element_type=jnp.float32)
    sigmoid_gate = jax.nn.sigmoid(gate_pre)
    active = gate_pre * sigmoid_gate
    hidden = active * up_pre
    scaled_back = gate_rows * back_proj
    d_gate = (scaled_back * up_pre * sigmoid_gate * (1.0 + gate_pre * (1.0 - sigmoid_gate))).astype(
        jnp.bfloat16
    )
    d_up = (scaled_back * active).astype(jnp.bfloat16)
    scaled_hidden = (gate_rows * hidden).astype(jnp.bfloat16)
    gate_terms = jnp.sum(back_proj * hidden, axis=-1)

    row_count = x_rows.shape[0]
    first_slot = (jnp.arange(row_count, dtype=jnp.int32) % REPS == 0)[:, None]

    def by_slot(d):
        zero = jnp.zeros((), d.dtype)
        return jnp.concatenate([jnp.where(first_slot, d, zero), jnp.where(first_slot, zero, d)], axis=1)

    def slot_pair_sum(rows, d):
        acc = jnp.einsum("rd,rh->dh", rows, by_slot(d), preferred_element_type=jnp.float32)
        acc = lax.reduce_precision(acc, exponent_bits=8, mantissa_bits=7)
        return (acc[:, :half] + acc[:, half:]).astype(jnp.bfloat16)

    grad_gate_cols = slot_pair_sum(x_rows, d_gate)
    grad_up_cols = slot_pair_sum(x_rows, d_up)
    grad_down_cols = slot_pair_sum(dy_rows, scaled_hidden)

    pad_rows = ((0, LANE), (0, 0))
    row_ext = jnp.einsum("rh,dh->rd", d_gate, jnp.pad(slot_gate, pad_rows), preferred_element_type=jnp.float32)
    row_ext = row_ext + jnp.einsum(
        "rh,dh->rd", d_up, jnp.pad(slot_up, pad_rows), preferred_element_type=jnp.float32
    )
    term_col = jnp.arange(wide, dtype=jnp.int32)[None, :] == model_width
    row_ext = row_ext + jnp.where(term_col, gate_terms[:, None], 0.0)

    summed = lax.psum_scatter(row_ext, "node", scatter_dimension=0, tiled=True)
    back = lax.all_to_all(summed.reshape(col_count, per_rank, wide), "dev", 0, 0, tiled=True)
    back = jnp.sum(back.reshape(round_total, REPS, per_rank, wide), axis=1).reshape(row_slots, wide)

    grad_tokens = jnp.einsum(
        "qt,qd->td",
        pick_rows,
        back[:, :model_width],
        precision=lax.Precision.HIGH,
    ).astype(jnp.bfloat16)
    back_q = back[:, model_width]
    rank_back = jnp.sum(jnp.where(chooser, back_q[:, None, None], 0.0), axis=0)
    grad_gates = jnp.sum(jnp.where(match, rank_back[:, None, :], 0.0), axis=-1)

    def home(cols):
        sent = cols.reshape(col_count, chunk, half)
        got = lax.all_to_all(sent, "dev", 0, 0, tiled=True).reshape(round_total, REPS, chunk, half)
        return jnp.concatenate([got[:, h] for h in range(REPS)], axis=-1)

    grad_w_gate = home(grad_gate_cols)
    grad_w_up = home(grad_up_cols)
    got_down = lax.all_to_all(grad_down_cols.reshape(col_count, chunk, half), "dev", 0, 0, tiled=True)
    got_down = got_down.reshape(round_total, REPS, chunk, half)
    grad_w_down = jnp.concatenate([jnp.swapaxes(got_down[:, h], 1, 2) for h in range(REPS)], axis=1)
    del node_count
    return (grad_tokens, grad_gates, grad_w_gate, grad_w_up, grad_w_down)


def solution(mesh):
    return jax.shard_map(
        local,
        mesh=mesh,
        in_specs=(
            P(("node", "dev"), None),
            P(("node", "dev"), None),
            P(("node", "dev"), None),
            P(("node", "dev"), None),
            P(),
            P(None, "dev", "node"),
            P(None, "dev", "node"),
            P(None, "node", "dev"),
        ),
        out_specs=(
            P(("node", "dev"), None),
            P(("node", "dev"), None),
            P(None, "dev", "node"),
            P(None, "dev", "node"),
            P(None, "node", "dev"),
        ),
        check_vma=False,
    )
```

```python
import jax
import jax.numpy as jnp
from jax import lax
from jax.sharding import PartitionSpec as P


CAP = 2
REPS = 2
LANE = 128


def routing(expert_ids, slot_plan, slot_count, round_total):
    expert_count = slot_plan.shape[0]
    in_round = (slot_plan[:, 0] < slot_count).astype(jnp.int32)
    expert_rank = jnp.cumsum(in_round) - 1
    rank_match = (in_round[:, None] > 0) & (
        expert_rank[:, None] == jnp.arange(round_total, dtype=jnp.int32)[None, :]
    )
    hot_ids = jnp.sum(
        jnp.where(rank_match, jnp.arange(expert_count, dtype=jnp.int32)[:, None], 0), axis=0
    )
    match = expert_ids[:, :, None] == hot_ids[None, None, :]
    named = jnp.sum(match.astype(jnp.int32), axis=1)
    tok_rows = expert_ids.shape[0]
    earlier = (
        jnp.arange(tok_rows, dtype=jnp.int32)[None, :] < jnp.arange(tok_rows, dtype=jnp.int32)[:, None]
    ).astype(jnp.bfloat16)
    before = jnp.dot(earlier, named.astype(jnp.bfloat16), preferred_element_type=jnp.float32).astype(
        jnp.int32
    )
    per_rank = REPS * CAP
    target = per_rank * jnp.arange(round_total, dtype=jnp.int32)[None, :] + before
    return match, named, target


def local(tokens, grad_out, router_gates, expert_ids, slot_plan, w_gate, w_up, w_down):
    col_count = lax.axis_size("dev")
    node_count = lax.axis_size("node")
    _, model_width = tokens.shape
    round_total, chunk, node_hidden = w_gate.shape
    half = node_hidden // REPS
    per_rank = REPS * CAP
    row_slots = round_total * per_rank
    wide = model_width + LANE

    def split_cols(w):
        w = w.reshape(round_total, chunk, REPS, half)
        return jnp.swapaxes(w, 1, 2).reshape(col_count, chunk, half)

    send_wg = split_cols(w_gate)
    send_wu = split_cols(w_up)
    send_wd = split_cols(jnp.swapaxes(w_down, 1, 2))
    slot_gate = lax.all_to_all(send_wg, "dev", 0, 0, tiled=True).reshape(model_width, half)
    slot_up = lax.all_to_all(send_wu, "dev", 0, 0, tiled=True).reshape(model_width, half)
    slot_down_t = lax.all_to_all(send_wd, "dev", 0, 0, tiled=True).reshape(model_width, half)

    match, named, target = routing(expert_ids, slot_plan, col_count, round_total)
    q_ids = jnp.arange(row_slots, dtype=jnp.int32)
    chooser = (named[None, :, :] > 0) & (target[None, :, :] == q_ids[:, None, None])
    pick_rows = jnp.sum(chooser.astype(jnp.float32), axis=-1)
    pick_half = pick_rows.astype(jnp.bfloat16)
    gates_f = router_gates.astype(jnp.float32)
    rank_gate = jnp.sum(jnp.where(match, gates_f[:, :, None], 0.0), axis=1)
    gate_send = jnp.sum(jnp.where(chooser, rank_gate[None, :, :], 0.0), axis=(1, 2)).astype(jnp.bfloat16)

    x_send = jnp.dot(pick_half, tokens, preferred_element_type=jnp.float32).astype(jnp.bfloat16)
    dy_send = jnp.dot(pick_half, grad_out, preferred_element_type=jnp.float32).astype(jnp.bfloat16)
    gate_block = jnp.zeros((row_slots, LANE), jnp.bfloat16).at[:, 0].set(gate_send)
    dy_send = jnp.concatenate([dy_send, gate_block], axis=1)

    both_send = jnp.concatenate([x_send, dy_send], axis=1)
    both_width = model_width + wide
    both = both_send.reshape(round_total, 1, per_rank, both_width)
    both = jnp.broadcast_to(both, (round_total, REPS, per_rank, both_width))
    both = lax.all_to_all(both.reshape(col_count, per_rank, both_width), "dev", 0, 0, tiled=True)
    both = both.reshape(col_count * per_rank, both_width)
    x_rows = lax.all_gather(both[:, :model_width], "node", axis=0, tiled=True)
    dy_ext = lax.all_gather(both[:, model_width:], "node", axis=0, tiled=True)
    dy_rows = dy_ext[:, :model_width]
    gate_rows = dy_ext[:, model_width].astype(jnp.float32)[:, None]

    gate_pre = jnp.dot(x_rows, slot_gate, preferred_element_type=jnp.float32)
    up_pre = jnp.dot(x_rows, slot_up, preferred_element_type=jnp.float32)
    back_proj = jnp.dot(dy_rows, slot_down_t, preferred_element_type=jnp.float32)
    sigmoid_gate = jax.nn.sigmoid(gate_pre)
    active = gate_pre * sigmoid_gate
    hidden = active * up_pre
    scaled_back = gate_rows * back_proj
    d_gate = (scaled_back * up_pre * sigmoid_gate * (1.0 + gate_pre * (1.0 - sigmoid_gate))).astype(
        jnp.bfloat16
    )
    d_up = (scaled_back * active).astype(jnp.bfloat16)
    scaled_hidden = (gate_rows * hidden).astype(jnp.bfloat16)
    gate_terms = jnp.sum(back_proj * hidden, axis=-1)

    row_count = x_rows.shape[0]
    first_slot = (jnp.arange(row_count, dtype=jnp.int32) % REPS == 0)[:, None]

    def by_slot(d):
        zero = jnp.zeros((), d.dtype)
        return jnp.concatenate([jnp.where(first_slot, d, zero), jnp.where(first_slot, zero, d)], axis=1)

    def slot_pair_sum(rows, d):
        acc = jnp.einsum("rd,rh->dh", rows, by_slot(d), preferred_element_type=jnp.float32)
        acc = lax.reduce_precision(acc, exponent_bits=8, mantissa_bits=7)
        return (acc[:, :half] + acc[:, half:]).astype(jnp.bfloat16)

    grad_gate_cols = slot_pair_sum(x_rows, d_gate)
    grad_up_cols = slot_pair_sum(x_rows, d_up)
    grad_down_cols = slot_pair_sum(dy_rows, scaled_hidden)

    pad_rows = ((0, LANE), (0, 0))
    row_ext = jnp.einsum("rh,dh->rd", d_gate, jnp.pad(slot_gate, pad_rows), preferred_element_type=jnp.float32)
    row_ext = row_ext + jnp.einsum(
        "rh,dh->rd", d_up, jnp.pad(slot_up, pad_rows), preferred_element_type=jnp.float32
    )
    term_col = jnp.arange(wide, dtype=jnp.int32)[None, :] == model_width
    row_ext = row_ext + jnp.where(term_col, gate_terms[:, None], 0.0)

    summed = lax.psum_scatter(row_ext, "node", scatter_dimension=0, tiled=True)
    back = lax.all_to_all(summed.reshape(col_count, per_rank, wide), "dev", 0, 0, tiled=True)
    back = jnp.sum(back.reshape(round_total, REPS, per_rank, wide), axis=1).reshape(row_slots, wide)

    grad_tokens = jnp.einsum(
        "qt,qd->td",
        pick_rows,
        back[:, :model_width],
        precision=lax.Precision.HIGH,
    ).astype(jnp.bfloat16)
    back_q = back[:, model_width]
    rank_back = jnp.sum(jnp.where(chooser, back_q[:, None, None], 0.0), axis=0)
    grad_gates = jnp.sum(jnp.where(match, rank_back[:, None, :], 0.0), axis=-1)

    def home(cols):
        sent = cols.reshape(col_count, chunk, half)
        got = lax.all_to_all(sent, "dev", 0, 0, tiled=True)
        got = got.reshape(round_total, REPS, chunk, half)
        return jnp.concatenate([got[:, h] for h in range(REPS)], axis=-1)

    grad_w_gate = home(grad_gate_cols)
    grad_w_up = home(grad_up_cols)
    got_down = lax.all_to_all(grad_down_cols.reshape(col_count, chunk, half), "dev", 0, 0, tiled=True)
    got_down = got_down.reshape(round_total, REPS, chunk, half)
    grad_w_down = jnp.concatenate([jnp.swapaxes(got_down[:, h], 1, 2) for h in range(REPS)], axis=1)
    del node_count
    return (grad_tokens, grad_gates, grad_w_gate, grad_w_up, grad_w_down)


def solution(mesh):
    return jax.shard_map(
        local,
        mesh=mesh,
        in_specs=(
            P(("node", "dev"), None),
            P(("node", "dev"), None),
            P(("node", "dev"), None),
            P(("node", "dev"), None),
            P(),
            P(None, "dev", "node"),
            P(None, "dev", "node"),
            P(None, "node", "dev"),
        ),
        out_specs=(
            P(("node", "dev"), None),
            P(("node", "dev"), None),
            P(None, "dev", "node"),
            P(None, "dev", "node"),
            P(None, "node", "dev"),
        ),
        check_vma=False,
    )
```

```python
import jax
import jax.numpy as jnp
from jax import lax
from jax.sharding import PartitionSpec as P

TOP = 8
CAP = 2
REPS = 2
LANE = 128


def routing(expert_ids, slot_plan, slot_count, round_total):
    expert_count = slot_plan.shape[0]
    in_round = (slot_plan[:, 0] < slot_count).astype(jnp.int32)
    expert_rank = jnp.cumsum(in_round) - 1
    rank_match = (in_round[:, None] > 0) & (
        expert_rank[:, None] == jnp.arange(round_total, dtype=jnp.int32)[None, :]
    )
    hot_ids = jnp.sum(
        jnp.where(rank_match, jnp.arange(expert_count, dtype=jnp.int32)[:, None], 0), axis=0
    )
    match = expert_ids[:, :, None] == hot_ids[None, None, :]
    named = jnp.sum(match.astype(jnp.int32), axis=1)
    tok_rows = expert_ids.shape[0]
    earlier = (
        jnp.arange(tok_rows, dtype=jnp.int32)[None, :] < jnp.arange(tok_rows, dtype=jnp.int32)[:, None]
    ).astype(jnp.bfloat16)
    before = jnp.dot(earlier, named.astype(jnp.bfloat16), preferred_element_type=jnp.float32).astype(
        jnp.int32
    )
    per_rank = REPS * CAP
    target = per_rank * jnp.arange(round_total, dtype=jnp.int32)[None, :] + before
    return match, named, target


def local(tokens, grad_out, router_gates, expert_ids, slot_plan, w_gate, w_up, w_down):
    col_count = lax.axis_size("dev")
    node_count = lax.axis_size("node")
    tok_rows, model_width = tokens.shape
    round_total, chunk, node_hidden = w_gate.shape
    half = node_hidden // REPS
    per_rank = REPS * CAP
    row_slots = round_total * per_rank
    wide = model_width + LANE

    def split_cols(w):
        w = w.reshape(round_total, chunk, REPS, half)
        return jnp.swapaxes(w, 1, 2).reshape(col_count, chunk, half)

    send_wg = split_cols(w_gate)
    send_wu = split_cols(w_up)
    send_wd = split_cols(jnp.swapaxes(w_down, 1, 2))
    slot_gate = lax.all_to_all(send_wg, "dev", 0, 0, tiled=True).reshape(model_width, half)
    slot_up = lax.all_to_all(send_wu, "dev", 0, 0, tiled=True).reshape(model_width, half)
    slot_down_t = lax.all_to_all(send_wd, "dev", 0, 0, tiled=True).reshape(model_width, half)

    match, named, target = routing(expert_ids, slot_plan, col_count, round_total)
    q_ids = jnp.arange(row_slots, dtype=jnp.int32)
    chooser = (named[None, :, :] > 0) & (target[None, :, :] == q_ids[:, None, None])
    pick_rows = jnp.sum(chooser.astype(jnp.float32), axis=-1)
    pick_half = pick_rows.astype(jnp.bfloat16)
    gates_f = router_gates.astype(jnp.float32)
    rank_gate = jnp.sum(jnp.where(match, gates_f[:, :, None], 0.0), axis=1)
    gate_send = jnp.sum(jnp.where(chooser, rank_gate[None, :, :], 0.0), axis=(1, 2)).astype(jnp.bfloat16)

    x_send = jnp.dot(pick_half, tokens, preferred_element_type=jnp.float32).astype(jnp.bfloat16)
    dy_send = jnp.dot(pick_half, grad_out, preferred_element_type=jnp.float32).astype(jnp.bfloat16)
    gate_block = jnp.where(jnp.arange(LANE)[None, :] == 0, gate_send[:, None], jnp.zeros((), jnp.bfloat16))
    dy_send = jnp.concatenate([dy_send, gate_block], axis=1)

    both_send = jnp.concatenate([x_send, dy_send], axis=1)
    both_width = model_width + wide
    both = both_send.reshape(round_total, 1, per_rank, both_width)
    both = jnp.broadcast_to(both, (round_total, REPS, per_rank, both_width))
    both = lax.all_to_all(both.reshape(col_count, per_rank, both_width), "dev", 0, 0, tiled=True)
    both = both.reshape(col_count * per_rank, both_width)
    x_rows = lax.all_gather(both[:, :model_width], "node", axis=0, tiled=True)
    dy_ext = lax.all_gather(both[:, model_width:], "node", axis=0, tiled=True)
    dy_rows = dy_ext[:, :model_width]
    gate_rows = dy_ext[:, model_width].astype(jnp.float32)[:, None]

    gate_pre = jnp.dot(x_rows, slot_gate, preferred_element_type=jnp.float32)
    up_pre = jnp.dot(x_rows, slot_up, preferred_element_type=jnp.float32)
    back_proj = jnp.dot(dy_rows, slot_down_t, preferred_element_type=jnp.float32)
    sigmoid_gate = jax.nn.sigmoid(gate_pre)
    active = gate_pre * sigmoid_gate
    hidden = active * up_pre
    scaled_back = gate_rows * back_proj
    d_gate = (scaled_back * up_pre * sigmoid_gate * (1.0 + gate_pre * (1.0 - sigmoid_gate))).astype(
        jnp.bfloat16
    )
    d_up = (scaled_back * active).astype(jnp.bfloat16)
    scaled_hidden = (gate_rows * hidden).astype(jnp.bfloat16)
    gate_terms = jnp.sum(back_proj * hidden, axis=-1)

    row_count = x_rows.shape[0]
    first_slot = (jnp.arange(row_count, dtype=jnp.int32) % REPS == 0)[:, None]

    def by_slot(d):
        zero = jnp.zeros((), d.dtype)
        return jnp.concatenate([jnp.where(first_slot, d, zero), jnp.where(first_slot, zero, d)], axis=1)

    def slot_pair_sum(rows, d):
        acc = jnp.einsum("rd,rh->dh", rows, by_slot(d), preferred_element_type=jnp.float32)
        acc = lax.reduce_precision(acc, exponent_bits=8, mantissa_bits=7)
        return (acc[:, :half] + acc[:, half:]).astype(jnp.bfloat16)

    grad_gate_cols = slot_pair_sum(x_rows, d_gate)
    grad_up_cols = slot_pair_sum(x_rows, d_up)
    grad_down_cols = slot_pair_sum(dy_rows, scaled_hidden)

    pad_rows = ((0, LANE), (0, 0))
    row_ext = jnp.einsum("rh,dh->rd", d_gate, jnp.pad(slot_gate, pad_rows), preferred_element_type=jnp.float32)
    row_ext = row_ext + jnp.einsum(
        "rh,dh->rd", d_up, jnp.pad(slot_up, pad_rows), preferred_element_type=jnp.float32
    )
    term_col = jnp.arange(wide, dtype=jnp.int32)[None, :] == model_width
    row_ext = row_ext + jnp.where(term_col, gate_terms[:, None], 0.0)

    summed = lax.psum_scatter(row_ext, "node", scatter_dimension=0, tiled=True)
    back = lax.all_to_all(summed.reshape(col_count, per_rank, wide), "dev", 0, 0, tiled=True)
    back = jnp.sum(back.reshape(round_total, REPS, per_rank, wide), axis=1).reshape(row_slots, wide)

    back_tok = back[:, :model_width]
    back_hi = back_tok.astype(jnp.bfloat16)
    back_lo = (back_tok - back_hi.astype(jnp.float32)).astype(jnp.bfloat16)
    grad_tokens = jnp.einsum("qt,qd->td", pick_half, back_hi, preferred_element_type=jnp.float32)
    grad_tokens = grad_tokens + jnp.einsum("qt,qd->td", pick_half, back_lo, preferred_element_type=jnp.float32)
    grad_tokens = grad_tokens.astype(jnp.bfloat16)
    back_q = back[:, model_width]
    rank_back = jnp.sum(jnp.where(chooser, back_q[:, None, None], 0.0), axis=0)
    grad_gates = jnp.sum(jnp.where(match, rank_back[:, None, :], 0.0), axis=-1)

    def home(cols):
        sent = cols.reshape(col_count, chunk, half)
        got = lax.all_to_all(sent, "dev", 0, 0, tiled=True).reshape(round_total, REPS, chunk, half)
        return jnp.concatenate([got[:, h] for h in range(REPS)], axis=-1)

    grad_w_gate = home(grad_gate_cols)
    grad_w_up = home(grad_up_cols)
    got_down = lax.all_to_all(grad_down_cols.reshape(col_count, chunk, half), "dev", 0, 0, tiled=True)
    got_down = got_down.reshape(round_total, REPS, chunk, half)
    grad_w_down = jnp.concatenate([jnp.swapaxes(got_down[:, h], 1, 2) for h in range(REPS)], axis=1)
    del node_count
    return (grad_tokens, grad_gates, grad_w_gate, grad_w_up, grad_w_down)


def solution(mesh):
    return jax.shard_map(
        local,
        mesh=mesh,
        in_specs=(
            P(("node", "dev"), None),
            P(("node", "dev"), None),
            P(("node", "dev"), None),
            P(("node", "dev"), None),
            P(),
            P(None, "dev", "node"),
            P(None, "dev", "node"),
            P(None, "node", "dev"),
        ),
        out_specs=(
            P(("node", "dev"), None),
            P(("node", "dev"), None),
            P(None, "dev", "node"),
            P(None, "dev", "node"),
            P(None, "node", "dev"),
        ),
        check_vma=False,
    )
```

```python
import jax
import jax.numpy as jnp
from jax import lax
from jax.sharding import PartitionSpec as P

TOP = 8
CAP = 2
REPS = 2
LANE = 128


def routing(expert_ids, slot_plan, slot_count, round_total):
    expert_count = slot_plan.shape[0]
    in_round = (slot_plan[:, 0] < slot_count).astype(jnp.int32)
    expert_rank = jnp.cumsum(in_round) - 1
    rank_match = (in_round[:, None] > 0) & (
        expert_rank[:, None] == jnp.arange(round_total, dtype=jnp.int32)[None, :]
    )
    hot_ids = jnp.sum(
        jnp.where(rank_match, jnp.arange(expert_count, dtype=jnp.int32)[:, None], 0), axis=0
    )
    match = expert_ids[:, :, None] == hot_ids[None, None, :]
    named = jnp.sum(match.astype(jnp.int32), axis=1)
    tok_rows = expert_ids.shape[0]
    earlier = (
        jnp.arange(tok_rows, dtype=jnp.int32)[None, :] < jnp.arange(tok_rows, dtype=jnp.int32)[:, None]
    ).astype(jnp.bfloat16)
    before = jnp.dot(earlier, named.astype(jnp.bfloat16), preferred_element_type=jnp.float32).astype(
        jnp.int32
    )
    per_rank = REPS * CAP
    target = per_rank * jnp.arange(round_total, dtype=jnp.int32)[None, :] + before
    return match, named, target


def local(tokens, grad_out, router_gates, expert_ids, slot_plan, w_gate, w_up, w_down):
    col_count = lax.axis_size("dev")
    node_count = lax.axis_size("node")
    tok_rows, model_width = tokens.shape
    round_total, chunk, node_hidden = w_gate.shape
    half = node_hidden // REPS
    per_rank = REPS * CAP
    row_slots = round_total * per_rank
    wide = model_width + LANE

    def split_cols(w):
        w = w.reshape(round_total, chunk, REPS, half)
        return jnp.swapaxes(w, 1, 2).reshape(col_count, chunk, half)

    send_wg = split_cols(w_gate)
    send_wu = split_cols(w_up)
    send_wd = split_cols(jnp.swapaxes(w_down, 1, 2))
    slot_gate = lax.all_to_all(send_wg, "dev", 0, 0, tiled=True).reshape(model_width, half)
    slot_up = lax.all_to_all(send_wu, "dev", 0, 0, tiled=True).reshape(model_width, half)
    slot_down_t = lax.all_to_all(send_wd, "dev", 0, 0, tiled=True).reshape(model_width, half)

    match, named, target = routing(expert_ids, slot_plan, col_count, round_total)
    q_ids = jnp.arange(row_slots, dtype=jnp.int32)
    chooser = (named[None, :, :] > 0) & (target[None, :, :] == q_ids[:, None, None])
    pick_rows = jnp.sum(chooser.astype(jnp.float32), axis=-1)
    pick_half = pick_rows.astype(jnp.bfloat16)
    gates_f = router_gates.astype(jnp.float32)
    rank_gate = jnp.sum(jnp.where(match, gates_f[:, :, None], 0.0), axis=1)
    gate_send = jnp.sum(jnp.where(chooser, rank_gate[None, :, :], 0.0), axis=(1, 2)).astype(jnp.bfloat16)

    x_send = jnp.dot(pick_half, tokens, preferred_element_type=jnp.float32).astype(jnp.bfloat16)
    dy_send = jnp.dot(pick_half, grad_out, preferred_element_type=jnp.float32).astype(jnp.bfloat16)
    gate_block = jnp.where(jnp.arange(LANE)[None, :] == 0, gate_send[:, None], jnp.zeros((), jnp.bfloat16))
    dy_send = jnp.concatenate([dy_send, gate_block], axis=1)

    both_send = jnp.concatenate([x_send, dy_send], axis=1)
    both_width = model_width + wide
    both = both_send.reshape(round_total, 1, per_rank, both_width)
    both = jnp.broadcast_to(both, (round_total, REPS, per_rank, both_width))
    both = lax.all_to_all(both.reshape(col_count, per_rank, both_width), "dev", 0, 0, tiled=True)
    both = both.reshape(col_count * per_rank, both_width)
    x_rows = lax.all_gather(both[:, :model_width], "node", axis=0, tiled=True)
    dy_ext = lax.all_gather(both[:, model_width:], "node", axis=0, tiled=True)
    dy_rows = dy_ext[:, :model_width]
    gate_rows = dy_ext[:, model_width].astype(jnp.float32)[:, None]

    gate_pre = jnp.dot(x_rows, slot_gate, preferred_element_type=jnp.float32)
    up_pre = jnp.dot(x_rows, slot_up, preferred_element_type=jnp.float32)
    back_proj = jnp.dot(dy_rows, slot_down_t, preferred_element_type=jnp.float32)
    sigmoid_gate = jax.nn.sigmoid(gate_pre)
    active = gate_pre * sigmoid_gate
    hidden = active * up_pre
    scaled_back = gate_rows * back_proj
    d_gate = (scaled_back * up_pre * sigmoid_gate * (1.0 + gate_pre * (1.0 - sigmoid_gate))).astype(
        jnp.bfloat16
    )
    d_up = (scaled_back * active).astype(jnp.bfloat16)
    scaled_hidden = (gate_rows * hidden).astype(jnp.bfloat16)
    gate_terms = jnp.sum(back_proj * hidden, axis=-1)

    row_count = x_rows.shape[0]
    first_slot = (jnp.arange(row_count, dtype=jnp.int32) % REPS == 0)[:, None]

    def by_slot(d):
        zero = jnp.zeros((), d.dtype)
        return jnp.concatenate([jnp.where(first_slot, d, zero), jnp.where(first_slot, zero, d)], axis=1)

    def slot_pair_sum(rows, d):
        acc = jnp.einsum("rd,rh->dh", rows, by_slot(d), preferred_element_type=jnp.float32)
        acc = lax.reduce_precision(acc, exponent_bits=8, mantissa_bits=7)
        return (acc[:, :half] + acc[:, half:]).astype(jnp.bfloat16)

    grad_gate_cols = slot_pair_sum(x_rows, d_gate)
    grad_up_cols = slot_pair_sum(x_rows, d_up)
    grad_down_cols = slot_pair_sum(dy_rows, scaled_hidden)

    pad_rows = ((0, LANE), (0, 0))
    row_ext = jnp.einsum("rh,dh->rd", d_gate, jnp.pad(slot_gate, pad_rows), preferred_element_type=jnp.float32)
    row_ext = row_ext + jnp.einsum(
        "rh,dh->rd", d_up, jnp.pad(slot_up, pad_rows), preferred_element_type=jnp.float32
    )
    term_col = jnp.arange(wide, dtype=jnp.int32)[None, :] == model_width
    row_ext = row_ext + jnp.where(term_col, gate_terms[:, None], 0.0)

    summed = lax.psum_scatter(row_ext, "node", scatter_dimension=0, tiled=True)
    back = lax.all_to_all(summed.reshape(col_count, per_rank, wide), "dev", 0, 0, tiled=True)
    back = jnp.sum(back.reshape(round_total, REPS, per_rank, wide), axis=1).reshape(row_slots, wide)

    back_tok = back[:, :model_width]
    back_top = lax.reduce_precision(back_tok, exponent_bits=8, mantissa_bits=7)
    back_hi = back_top.astype(jnp.bfloat16)
    back_lo = (back_tok - back_top).astype(jnp.bfloat16)
    grad_tokens = jnp.einsum("qt,qd->td", pick_half, back_hi, preferred_element_type=jnp.float32)
    grad_tokens = grad_tokens + jnp.einsum("qt,qd->td", pick_half, back_lo, preferred_element_type=jnp.float32)
    grad_tokens = grad_tokens.astype(jnp.bfloat16)
    back_q = back[:, model_width]
    rank_back = jnp.sum(jnp.where(chooser, back_q[:, None, None], 0.0), axis=0)
    grad_gates = jnp.sum(jnp.where(match, rank_back[:, None, :], 0.0), axis=-1)

    def home(cols):
        sent = cols.reshape(col_count, chunk, half)
        got = lax.all_to_all(sent, "dev", 0, 0, tiled=True).reshape(round_total, REPS, chunk, half)
        return jnp.concatenate([got[:, h] for h in range(REPS)], axis=-1)

    grad_w_gate = home(grad_gate_cols)
    grad_w_up = home(grad_up_cols)
    got_down = lax.all_to_all(grad_down_cols.reshape(col_count, chunk, half), "dev", 0, 0, tiled=True)
    got_down = got_down.reshape(round_total, REPS, chunk, half)
    grad_w_down = jnp.concatenate([jnp.swapaxes(got_down[:, h], 1, 2) for h in range(REPS)], axis=1)
    del node_count
    return (grad_tokens, grad_gates, grad_w_gate, grad_w_up, grad_w_down)


def solution(mesh):
    return jax.shard_map(
        local,
        mesh=mesh,
        in_specs=(
            P(("node", "dev"), None),
            P(("node", "dev"), None),
            P(("node", "dev"), None),
            P(("node", "dev"), None),
            P(),
            P(None, "dev", "node"),
            P(None, "dev", "node"),
            P(None, "node", "dev"),
        ),
        out_specs=(
            P(("node", "dev"), None),
            P(("node", "dev"), None),
            P(None, "dev", "node"),
            P(None, "dev", "node"),
            P(None, "node", "dev"),
        ),
        check_vma=False,
    )
```
